1024 devices in a mesh: band: 32 (over x_lo, z, core), pw: 32 (over x_hi, y).
Axes of the slice: x: 8 (x_hi: 4, x_lo: 2; x = x_hi * 2 + x_lo), y: 8, z: 8, core: 2. Of those that a mesh axis runs over, the one named last changes fastest.
Arguments:
- orbitals: float32 [2, 32, 110592], P(None, 'band', 'pw'), may hold values from -6 to 6
- pw_index: int32 [110592], P('pw'), may hold values from 0 to 27647, as said below
- potential: float32 [96, 96, 96], P(None, 'pw'), may hold values from -1 to 2
Outputs:
- applied: float32 [2, 32, 110592], P(None, 'band', 'pw')
- gram: float32 [2, 32, 32], P(None, 'band')
The draws below stay inside these ranges and needn't reach their ends.
Inputs may be any that keep to these rules, and one draw needn't show every extreme that they name: `pw_index`: entry j of each device's block of 3456 entries names one of cells 8 j to 8 j + 7 of that device's 3 x 96 x 96 slab, counted with the last dimension fastest.
All inputs are finite; a program needn't handle non-finite values.
Results may differ from the reference program's by a relative error of at most 0.000053.
Values sent between devices are 32-bit elements; how exact they have to be, the bound alone decides.
No kernel may reach another device: no remote copies, remote signals or barrier semaphores. Data moves between devices by JAX's collectives and lax.ppermute only.
A program may use at most 32 MiB of HBM per device.

```python
import jax
import jax.numpy as jnp
from jax import lax

GRID = 96
NPW = 110592
NPW_DEV = 3456
BANDS = 32


def draw_pw_index(key, part):
    position = jnp.arange(NPW, dtype=jnp.int32) % NPW_DEV
    offsets = jax.random.randint(key, (NPW,), 0, 8, dtype=jnp.int32)
    offsets = jnp.where(position == 0, 0, jnp.where(position == NPW_DEV - 1, 7, offsets))
    return (position * 8 + offsets).astype(jnp.int32)


def steps_of(rng, shape, shards, low, largest):
    gain = 1.0
    for dim, blocks in shards:
        draws = jax.random.uniform(jax.random.fold_in(jax.random.fold_in(rng, 6), dim), (blocks,), jnp.float32, low / len(shards), largest / len(shards))
        gain = gain * jnp.repeat(jnp.exp(draws), shape[dim] // blocks).reshape((-1,) + (1,) * (len(shape) - 1 - dim))
    return gain


def gaussian(rng, shape, scale, limit, pieces=(), kind=jnp.bfloat16):
    loudness = steps_of(rng, shape, pieces, -0.22, 0.18) if pieces else 1.0
    values = jax.random.normal(rng, shape, jnp.float32) * scale * loudness
    return jnp.minimum(jnp.maximum(values, -limit), limit).astype(kind)


def setup_inputs(seed: int = 0) -> dict:
    streams_of = jax.random.split(jax.random.key(seed), 4)
    orbitals = gaussian(streams_of[0], (2, BANDS, NPW), 1.0, 6.0, ((1, 32), (2, 32)), jnp.float32)
    pw_index = draw_pw_index(jax.random.fold_in(streams_of[3], 71), 0)
    potential = jnp.clip(-1.0 + 3.0 * jax.random.uniform(streams_of[2], (GRID, GRID, GRID), jnp.float32) ** steps_of(streams_of[2], (GRID, GRID, GRID), ((1, 32),), -0.2, 0.2), -1.0, 2.0)
    return dict(orbitals=orbitals, pw_index=pw_index, potential=potential)


def reference(orbitals, pw_index, potential):
    owner = (jnp.arange(NPW, dtype=jnp.int32) // NPW_DEV).astype(jnp.int32)
    cell = (pw_index + owner * (8 * NPW_DEV)).astype(jnp.int32)

    def one_orbital(rows):
        real_part, imag_part = rows
        zeros_grid = jnp.zeros((GRID ** 3,), real_part.dtype)
        grid_real = zeros_grid.at[cell].set(real_part).reshape(GRID, GRID, GRID)
        grid_imag = zeros_grid.at[cell].set(imag_part).reshape(GRID, GRID, GRID)
        spread = lax.complex(grid_real, grid_imag)
        field = jnp.fft.ifftn(spread) * potential
        transformed = jnp.fft.fftn(field).reshape(-1)[cell]
        return jnp.real(transformed), jnp.imag(transformed)

    out_real, out_imag = lax.map(one_orbital, (orbitals[0], orbitals[1]))
    applied = jnp.stack([out_real, out_imag])
    first, second = orbitals[0], orbitals[1]
    highest = lax.Precision.HIGHEST
    gram_real = jnp.dot(first, first.T, precision=highest) + jnp.dot(second, second.T, precision=highest)
    gram_imag = jnp.dot(first, second.T, precision=highest) - jnp.dot(second, first.T, precision=highest)
    gram_matrix = jnp.stack([gram_real, gram_imag]) / NPW
    return applied, gram_matrix
```

```python
import math

import jax
import jax.numpy as jnp
from jax import lax
from jax.sharding import PartitionSpec as P

HIGHEST = lax.Precision.HIGHEST


def dft_table(length, inverse, rows, cols):
    indices = lax.iota(jnp.int32, length)
    product = indices[:, None] * indices[None, :] % length
    angles = product.astype(jnp.float32) * (2.0 * math.pi / length)
    cos, sin = jnp.cos(angles), jnp.sin(angles)
    if inverse:
        cos, sin = cos / length, sin / length
        table = jnp.stack([jnp.stack([cos, sin], 1), jnp.stack([-sin, cos], 1)], 0)
    else:
        table = jnp.stack([jnp.stack([cos, -sin], 1), jnp.stack([sin, cos], 1)], 0)
    perm_in = (0, 1) if rows == "ck" else (1, 0)
    perm_out = (2, 3) if cols == "dn" else (3, 2)
    table = jnp.transpose(table, perm_in + perm_out)
    return table.reshape(2 * length, 2 * length)


def contract(values, table, form):
    return jnp.einsum(form, values, table, precision=HIGHEST)


def gram_rows(orbitals):
    _, bands_here, columns = orbitals.shape
    n_band = lax.axis_size("band")
    n_pw = lax.axis_size("pw")
    chunk = columns // n_band
    pieces = orbitals.reshape(2, bands_here, n_band, chunk)
    pieces = lax.all_to_all(pieces, "band", split_axis=2, concat_axis=1, tiled=True)
    bands = bands_here * n_band
    stacked = pieces.reshape(2 * bands, chunk)
    prod = lax.dot_general(stacked, stacked, (((1,), (1,)), ((), ())), precision=HIGHEST)
    gram_real = prod[:bands, :bands] + prod[bands:, bands:]
    gram_imag = prod[:bands, bands:] - prod[bands:, :bands]
    partial = jnp.stack([gram_real, gram_imag]).reshape(1, 2, n_band, bands_here, bands)
    rows = lax.all_to_all(partial, "band", split_axis=2, concat_axis=0, tiled=True)
    rows = jnp.sum(rows, axis=0).reshape(1, 2, bands_here, bands)
    spread = jnp.broadcast_to(rows, (n_pw, 2, bands_here, bands))
    spread = lax.all_to_all(spread, "pw", split_axis=0, concat_axis=0, tiled=True)
    total = jnp.sum(spread, axis=0)
    return total / (columns * n_pw)


def local(orbitals, pw_index, potential):
    _, bands_here, columns = orbitals.shape
    grid = potential.shape[0]
    planes = potential.shape[1]
    blocks = grid // 8
    offsets = (pw_index - 8 * lax.iota(jnp.int32, columns)).reshape(planes, grid, blocks)
    lanes = lax.iota(jnp.int32, 8)
    hit = offsets[..., None] == lanes

    coeffs = orbitals.reshape(2, bands_here, planes, grid, blocks)
    coeffs = jnp.transpose(coeffs, (1, 2, 3, 0, 4))
    spread = jnp.where(hit[None, :, :, None], coeffs[..., None], 0.0)
    spread = spread.reshape(bands_here, planes, grid, 2 * grid)

    slab = contract(spread, dft_table(grid, True, "ck", "dn"), "bxyw,wv->bxyv")
    slab = slab.reshape(bands_here, planes, 2 * grid, grid)
    slab = contract(slab, dft_table(grid, True, "kc", "dn"), "bxwz,wv->bxvz")
    slab = slab.reshape(bands_here, planes, 2, grid, grid)
    piece = lax.all_to_all(slab, "pw", split_axis=3, concat_axis=1, tiled=True)
    piece = piece.reshape(bands_here, 2 * grid, planes, grid)
    piece = contract(piece, dft_table(grid, True, "kc", "nd"), "bwyz,wv->bvyz")
    piece = piece.reshape(bands_here, grid, 2, planes, grid) * potential[None, :, None]
    piece = piece.reshape(bands_here, 2 * grid, planes, grid)
    piece = contract(piece, dft_table(grid, False, "kc", "nd"), "bwyz,wv->bvyz")
    piece = piece.reshape(bands_here, grid, 2, planes, grid)
    back = lax.all_to_all(piece, "pw", split_axis=1, concat_axis=3, tiled=True)
    back = back.reshape(bands_here, planes, 2 * grid, grid)
    back = contract(back, dft_table(grid, False, "ck", "nd"), "bxwz,wv->bxvz")
    back = back.reshape(bands_here, planes, grid, 2 * grid)
    back = contract(back, dft_table(grid, False, "ck", "dn"), "bxyw,wv->bxyv")
    back = back.reshape(bands_here, planes, grid, 2, blocks, 8)
    picked = jnp.sum(jnp.where(hit[None, :, :, None], back, 0.0), axis=-1)
    applied = jnp.transpose(picked, (3, 0, 1, 2, 4)).reshape(2, bands_here, columns)
    return (applied, gram_rows(orbitals))


def solution(mesh):
    placed = (P(None, "band", "pw"), P("pw"), P(None, "pw", None))
    return jax.shard_map(
        local,
        mesh=mesh,
        in_specs=placed,
        out_specs=(P(None, "band", "pw"), P(None, "band", None)),
        check_vma=False,
    )
```

```python
import math

import jax
import numpy as np
import jax.numpy as jnp
from jax import lax
from jax.sharding import PartitionSpec as P

HIGHEST = lax.Precision.HIGHEST


def dft_table(length, inverse, rows, cols):
    indices = np.arange(length)
    angles = (np.outer(indices, indices) % length) * (2.0 * np.pi / length)
    cos, sin = np.cos(angles), np.sin(angles)
    if inverse:
        cos, sin = cos / length, sin / length
        table = np.stack([np.stack([cos, sin], 1), np.stack([-sin, cos], 1)], 0)
    else:
        table = np.stack([np.stack([cos, -sin], 1), np.stack([sin, cos], 1)], 0)
    perm_in = (0, 1) if rows == "ck" else (1, 0)
    perm_out = (2, 3) if cols == "dn" else (3, 2)
    table = np.transpose(table, perm_in + perm_out)
    return jnp.asarray(table.reshape(2 * length, 2 * length).astype(np.float32))


def contract(values, table, form):
    return jnp.einsum(form, values, table, precision=HIGHEST)


def gram_rows(orbitals):
    _, bands_here, columns = orbitals.shape
    n_band = lax.axis_size("band")
    chunk = columns // n_band
    pieces = orbitals.reshape(2, bands_here, n_band, chunk)
    pieces = lax.all_to_all(pieces, "band", split_axis=2, concat_axis=1, tiled=True)
    bands = bands_here * n_band
    stacked = pieces.reshape(2 * bands, chunk)
    prod = lax.dot_general(stacked, stacked, (((1,), (1,)), ((), ())), precision=HIGHEST)
    gram_real = prod[:bands, :bands] + prod[bands:, bands:]
    gram_imag = prod[:bands, bands:] - prod[bands:, :bands]
    partial = jnp.stack([gram_real, gram_imag]).reshape(1, 2, n_band, bands_here, bands)
    rows = lax.all_to_all(partial, "band", split_axis=2, concat_axis=0, tiled=True)
    return jnp.sum(rows, axis=0).reshape(2, bands_here, bands)


def local(orbitals, pw_index, potential):
    _, bands_here, columns = orbitals.shape
    grid = potential.shape[0]
    planes = potential.shape[1]
    blocks = grid // 8
    offsets = (pw_index - 8 * lax.iota(jnp.int32, columns)).reshape(planes, grid, blocks)
    lanes = lax.iota(jnp.int32, 8)
    hit = offsets[..., None] == lanes
    rows = gram_rows(orbitals)

    coeffs = orbitals.reshape(2, bands_here, planes, grid, blocks)
    coeffs = jnp.transpose(coeffs, (1, 2, 3, 0, 4))
    spread = jnp.where(hit[None, :, :, None], coeffs[..., None], 0.0)
    spread = spread.reshape(bands_here, planes, grid, 2 * grid)

    slab = contract(spread, dft_table(grid, True, "ck", "dn"), "bxyw,wv->bxyv")
    slab = slab.reshape(bands_here, planes, 2 * grid, grid)
    slab = contract(slab, dft_table(grid, True, "kc", "dn"), "bxwz,wv->bxvz")
    slab = slab.reshape(bands_here, planes, 2, grid, grid)
    piece = lax.all_to_all(slab, "pw", split_axis=3, concat_axis=1, tiled=True)
    piece = piece.reshape(bands_here, 2 * grid, planes, grid)
    piece = contract(piece, dft_table(grid, True, "kc", "nd"), "bwyz,wv->bvyz")
    piece = piece.reshape(bands_here, grid, 2, planes, grid) * potential[None, :, None]
    piece = piece.reshape(bands_here, 2 * grid, planes, grid)
    piece = contract(piece, dft_table(grid, False, "kc", "nd"), "bwyz,wv->bvyz")
    n_pw = lax.axis_size("pw")
    width = planes * 2 * planes * grid
    payload = piece.reshape(bands_here, n_pw, width).transpose(1, 0, 2)
    payload = payload.reshape(n_pw, bands_here * width)
    extra = jnp.broadcast_to(rows.reshape(1, -1), (n_pw, rows.size))
    payload = jnp.concatenate([payload, extra], axis=1)
    payload = lax.all_to_all(payload, "pw", split_axis=0, concat_axis=0, tiled=True)
    gram = jnp.sum(payload[:, bands_here * width :], axis=0).reshape(rows.shape)
    gram = gram / (columns * n_pw)
    back = payload[:, : bands_here * width].reshape(n_pw, bands_here, planes, 2, planes, grid)
    back = jnp.transpose(back, (1, 2, 3, 0, 4, 5))
    back = back.reshape(bands_here, planes, 2 * grid, grid)
    back = contract(back, dft_table(grid, False, "ck", "nd"), "bxwz,wv->bxvz")
    back = back.reshape(bands_here, planes, grid, 2 * grid)
    back = contract(back, dft_table(grid, False, "ck", "dn"), "bxyw,wv->bxyv")
    back = back.reshape(bands_here, planes, grid, 2, blocks, 8)
    picked = jnp.sum(jnp.where(hit[None, :, :, None], back, 0.0), axis=-1)
    applied = jnp.transpose(picked, (3, 0, 1, 2, 4)).reshape(2, bands_here, columns)
    return (applied, gram)


def solution(mesh):
    placed = (P(None, "band", "pw"), P("pw"), P(None, "pw", None))
    return jax.shard_map(
        local,
        mesh=mesh,
        in_specs=placed,
        out_specs=(P(None, "band", "pw"), P(None, "band", None)),
        check_vma=False,
    )
```

```python
import math

import jax
import numpy as np
import jax.numpy as jnp
from jax import lax
from jax.sharding import PartitionSpec as P

HIGHEST = lax.Precision.HIGHEST


def dft_table(length, inverse, rows, cols):
    indices = np.arange(length)
    angles = (np.outer(indices, indices) % length) * (2.0 * np.pi / length)
    cos, sin = np.cos(angles), np.sin(angles)
    if inverse:
        cos, sin = cos / length, sin / length
        table = np.stack([np.stack([cos, sin], 1), np.stack([-sin, cos], 1)], 0)
    else:
        table = np.stack([np.stack([cos, -sin], 1), np.stack([sin, cos], 1)], 0)
    perm_in = (0, 1) if rows == "ck" else (1, 0)
    perm_out = (2, 3) if cols == "dn" else (3, 2)
    table = np.transpose(table, perm_in + perm_out)
    return jnp.asarray(table.reshape(2 * length, 2 * length).astype(np.float32))


def contract(values, table, form):
    return jnp.einsum(form, values, table, precision=HIGHEST)


def gram_rows(orbitals):
    _, bands_here, columns = orbitals.shape
    n_band = lax.axis_size("band")
    me = lax.axis_index("band")
    buffer = orbitals[None]
    step = 1
    while step < n_band:
        pairs = [(i, i ^ step) for i in range(n_band)]
        buffer = jnp.concatenate([buffer, lax.ppermute(buffer, "band", pairs)], axis=0)
        step *= 2
    prod = jnp.einsum("cbg,tefg->cbtfe", orbitals, buffer, precision=HIGHEST)
    gram_real = prod[0, ..., 0] + prod[1, ..., 1]
    gram_imag = prod[0, ..., 1] - prod[1, ..., 0]
    slots = jnp.stack([gram_real, gram_imag])
    held = lax.iota(jnp.int32, n_band) ^ me
    rows = jnp.take(slots, held, axis=2)
    return rows.reshape(2, bands_here, n_band * bands_here)


def local(orbitals, pw_index, potential):
    _, bands_here, columns = orbitals.shape
    grid = potential.shape[0]
    planes = potential.shape[1]
    blocks = grid // 8
    offsets = (pw_index - 8 * lax.iota(jnp.int32, columns)).reshape(planes, grid, blocks)
    lanes = lax.iota(jnp.int32, 8)
    hit = offsets[..., None] == lanes
    rows = gram_rows(orbitals)

    coeffs = orbitals.reshape(2, bands_here, planes, grid, blocks)
    coeffs = jnp.transpose(coeffs, (1, 2, 3, 0, 4))
    spread = jnp.where(hit[None, :, :, None], coeffs[..., None], 0.0)
    spread = spread.reshape(bands_here, planes, grid, 2 * grid)

    slab = contract(spread, dft_table(grid, True, "ck", "dn"), "bxyw,wv->bxyv")
    slab = slab.reshape(bands_here, planes, 2 * grid, grid)
    slab = contract(slab, dft_table(grid, True, "kc", "dn"), "bxwz,wv->bxvz")
    slab = slab.reshape(bands_here, planes, 2, grid, grid)
    piece = lax.all_to_all(slab, "pw", split_axis=3, concat_axis=1, tiled=True)
    piece = piece.reshape(bands_here, 2 * grid, planes, grid)
    piece = contract(piece, dft_table(grid, True, "kc", "nd"), "bwyz,wv->bvyz")
    piece = piece.reshape(bands_here, grid, 2, planes, grid) * potential[None, :, None]
    piece = piece.reshape(bands_here, 2 * grid, planes, grid)
    piece = contract(piece, dft_table(grid, False, "kc", "nd"), "bwyz,wv->bvyz")
    n_pw = lax.axis_size("pw")
    width = planes * 2 * planes * grid
    payload = piece.reshape(bands_here, n_pw, width).transpose(1, 0, 2)
    payload = payload.reshape(n_pw, bands_here * width)
    extra = jnp.broadcast_to(rows.reshape(1, -1), (n_pw, rows.size))
    payload = jnp.concatenate([payload, extra], axis=1)
    payload = lax.all_to_all(payload, "pw", split_axis=0, concat_axis=0, tiled=True)
    gram = jnp.sum(payload[:, bands_here * width :], axis=0).reshape(rows.shape)
    gram = gram / (columns * n_pw)
    back = payload[:, : bands_here * width].reshape(n_pw, bands_here, planes, 2, planes, grid)
    back = jnp.transpose(back, (1, 2, 3, 0, 4, 5))
    back = back.reshape(bands_here, planes, 2 * grid, grid)
    back = contract(back, dft_table(grid, False, "ck", "nd"), "bxwz,wv->bxvz")
    back = back.reshape(bands_here, planes, grid, 2 * grid)
    back = contract(back, dft_table(grid, False, "ck", "dn"), "bxyw,wv->bxyv")
    back = back.reshape(bands_here, planes, grid, 2, blocks, 8)
    picked = jnp.sum(jnp.where(hit[None, :, :, None], back, 0.0), axis=-1)
    applied = jnp.transpose(picked, (3, 0, 1, 2, 4)).reshape(2, bands_here, columns)
    return (applied, gram)


def solution(mesh):
    placed = (P(None, "band", "pw"), P("pw"), P(None, "pw", None))
    return jax.shard_map(
        local,
        mesh=mesh,
        in_specs=placed,
        out_specs=(P(None, "band", "pw"), P(None, "band", None)),
        check_vma=False,
    )
```

```python
import math

import jax
import numpy as np
import jax.numpy as jnp
from jax import lax
from jax.sharding import PartitionSpec as P

HIGHEST = lax.Precision.HIGHEST


def dft_table(length, inverse, rows, cols):
    indices = np.arange(length)
    angles = (np.outer(indices, indices) % length) * (2.0 * np.pi / length)
    cos, sin = np.cos(angles), np.sin(angles)
    if inverse:
        cos, sin = cos / length, sin / length
        table = np.stack([np.stack([cos, sin], 1), np.stack([-sin, cos], 1)], 0)
    else:
        table = np.stack([np.stack([cos, -sin], 1), np.stack([sin, cos], 1)], 0)
    perm_in = (0, 1) if rows == "ck" else (1, 0)
    perm_out = (2, 3) if cols == "dn" else (3, 2)
    table = np.transpose(table, perm_in + perm_out)
    return jnp.asarray(table.reshape(2 * length, 2 * length).astype(np.float32))


def contract(values, table, form):
    return jnp.einsum(form, values, table, precision=HIGHEST)


def gram_rows(orbitals):
    _, bands_here, columns = orbitals.shape
    n_band = lax.axis_size("band")
    chunk = columns // n_band
    pieces = orbitals.reshape(2, bands_here, n_band, chunk)
    pieces = lax.all_to_all(pieces, "band", split_axis=2, concat_axis=1, tiled=True)
    bands = bands_here * n_band
    stacked = pieces.reshape(2 * bands, chunk)
    prod = lax.dot_general(stacked, stacked, (((1,), (1,)), ((), ())), precision=HIGHEST)
    gram_real = prod[:bands, :bands] + prod[bands:, bands:]
    gram_imag = prod[:bands, bands:] - prod[bands:, :bands]
    partial = jnp.stack([gram_real, gram_imag]).reshape(2, n_band, bands_here, bands)
    return scatter_rows(jnp.transpose(partial, (1, 0, 2, 3)))


def scatter_rows(blocks):
    n_band = blocks.shape[0]
    me = lax.axis_index("band")
    bits = n_band.bit_length() - 1
    assert 1 << bits == n_band
    buffer = blocks.reshape((2,) * bits + blocks.shape[1:])
    for bit in range(bits):
        axis = bits - 1 - bit
        mine = (me >> bit) & 1
        low = lax.index_in_dim(buffer, 0, axis, keepdims=False)
        high = lax.index_in_dim(buffer, 1, axis, keepdims=False)
        keep = jnp.where(mine == 1, high, low)
        send = jnp.where(mine == 1, low, high)
        pairs = [(i, i ^ (1 << bit)) for i in range(n_band)]
        buffer = keep + lax.ppermute(send, "band", pairs)
    return buffer


def local(orbitals, pw_index, potential):
    _, bands_here, columns = orbitals.shape
    grid = potential.shape[0]
    planes = potential.shape[1]
    blocks = grid // 8
    offsets = (pw_index - 8 * lax.iota(jnp.int32, columns)).reshape(planes, grid, blocks)
    lanes = lax.iota(jnp.int32, 8)
    hit = offsets[..., None] == lanes
    rows = gram_rows(orbitals)

    coeffs = orbitals.reshape(2, bands_here, planes, grid, blocks)
    coeffs = jnp.transpose(coeffs, (1, 2, 3, 0, 4))
    spread = jnp.where(hit[None, :, :, None], coeffs[..., None], 0.0)
    spread = spread.reshape(bands_here, planes, grid, 2 * grid)

    slab = contract(spread, dft_table(grid, True, "ck", "dn"), "bxyw,wv->bxyv")
    slab = slab.reshape(bands_here, planes, 2 * grid, grid)
    slab = contract(slab, dft_table(grid, True, "kc", "dn"), "bxwz,wv->bxvz")
    slab = slab.reshape(bands_here, planes, 2, grid, grid)
    piece = lax.all_to_all(slab, "pw", split_axis=3, concat_axis=1, tiled=True)
    piece = piece.reshape(bands_here, 2 * grid, planes, grid)
    piece = contract(piece, dft_table(grid, True, "kc", "nd"), "bwyz,wv->bvyz")
    piece = piece.reshape(bands_here, grid, 2, planes, grid) * potential[None, :, None]
    piece = piece.reshape(bands_here, 2 * grid, planes, grid)
    piece = contract(piece, dft_table(grid, False, "kc", "nd"), "bwyz,wv->bvyz")
    n_pw = lax.axis_size("pw")
    width = planes * 2 * planes * grid
    payload = piece.reshape(bands_here, n_pw, width).transpose(1, 0, 2)
    payload = payload.reshape(n_pw, bands_here * width)
    extra = jnp.broadcast_to(rows.reshape(1, -1), (n_pw, rows.size))
    payload = jnp.concatenate([payload, extra], axis=1)
    payload = lax.all_to_all(payload, "pw", split_axis=0, concat_axis=0, tiled=True)
    gram = jnp.sum(payload[:, bands_here * width :], axis=0).reshape(rows.shape)
    gram = gram / (columns * n_pw)
    back = payload[:, : bands_here * width].reshape(n_pw, bands_here, planes, 2, planes, grid)
    back = jnp.transpose(back, (1, 2, 3, 0, 4, 5))
    back = back.reshape(bands_here, planes, 2 * grid, grid)
    back = contract(back, dft_table(grid, False, "ck", "nd"), "bxwz,wv->bxvz")
    back = back.reshape(bands_here, planes, grid, 2 * grid)
    back = contract(back, dft_table(grid, False, "ck", "dn"), "bxyw,wv->bxyv")
    back = back.reshape(bands_here, planes, grid, 2, blocks, 8)
    picked = jnp.sum(jnp.where(hit[None, :, :, None], back, 0.0), axis=-1)
    applied = jnp.transpose(picked, (3, 0, 1, 2, 4)).reshape(2, bands_here, columns)
    return (applied, gram)


def solution(mesh):
    placed = (P(None, "band", "pw"), P("pw"), P(None, "pw", None))
    return jax.shard_map(
        local,
        mesh=mesh,
        in_specs=placed,
        out_specs=(P(None, "band", "pw"), P(None, "band", None)),
        check_vma=False,
    )
```

```python
import math

import jax
import numpy as np
import jax.numpy as jnp
from jax import lax
from jax.sharding import PartitionSpec as P

HIGHEST = lax.Precision.HIGHEST


def dft_table(length, inverse, rows, cols):
    indices = np.arange(length)
    angles = (np.outer(indices, indices) % length) * (2.0 * np.pi / length)
    cos, sin = np.cos(angles), np.sin(angles)
    if inverse:
        cos, sin = cos / length, sin / length
        table = np.stack([np.stack([cos, sin], 1), np.stack([-sin, cos], 1)], 0)
    else:
        table = np.stack([np.stack([cos, -sin], 1), np.stack([sin, cos], 1)], 0)
    perm_in = (0, 1) if rows == "ck" else (1, 0)
    perm_out = (2, 3) if cols == "dn" else (3, 2)
    table = np.transpose(table, perm_in + perm_out)
    return jnp.asarray(table.reshape(2 * length, 2 * length).astype(np.float32))


def contract(values, table, form):
    return jnp.einsum(form, values, table, precision=HIGHEST)


def exchange(blocks, axis):
    n = blocks.shape[0]
    flat = lax.all_to_all(blocks.reshape(n, -1), axis, split_axis=0, concat_axis=0, tiled=True)
    return flat.reshape(blocks.shape)


def gram_rows(orbitals):
    _, bands_here, columns = orbitals.shape
    n_band = lax.axis_size("band")
    chunk = columns // n_band
    pieces = jnp.transpose(orbitals.reshape(2, bands_here, n_band, chunk), (2, 0, 1, 3))
    pieces = exchange(pieces, "band")
    bands = bands_here * n_band
    stacked = jnp.transpose(pieces, (1, 0, 2, 3)).reshape(2 * bands, chunk)
    prod = lax.dot_general(stacked, stacked, (((1,), (1,)), ((), ())), precision=HIGHEST)
    gram_real = prod[:bands, :bands] + prod[bands:, bands:]
    gram_imag = prod[:bands, bands:] - prod[bands:, :bands]
    partial = jnp.stack([gram_real, gram_imag]).reshape(2, n_band, bands_here, bands)
    rows = exchange(jnp.transpose(partial, (1, 0, 2, 3)), "band")
    return jnp.sum(rows, axis=0)


def local(orbitals, pw_index, potential):
    _, bands_here, columns = orbitals.shape
    grid = potential.shape[0]
    planes = potential.shape[1]
    blocks = grid // 8
    offsets = (pw_index - 8 * lax.iota(jnp.int32, columns)).reshape(planes, grid, blocks)
    lanes = lax.iota(jnp.int32, 8)
    hit = offsets[..., None] == lanes

    coeffs = orbitals.reshape(2, bands_here, planes, grid, blocks)
    coeffs = jnp.transpose(coeffs, (1, 2, 3, 0, 4))
    spread = jnp.where(hit[None, :, :, None], coeffs[..., None], 0.0)
    spread = spread.reshape(bands_here, planes, grid, 2 * grid)

    slab = contract(spread, dft_table(grid, True, "ck", "dn"), "bxyw,wv->bxyv")
    slab = slab.reshape(bands_here, planes, 2 * grid, grid)
    slab = contract(slab, dft_table(grid, True, "kc", "dn"), "bxwz,wv->bxvz")
    slab, orbitals = lax.optimization_barrier((slab, orbitals))
    rows = gram_rows(orbitals)
    slab, rows = lax.optimization_barrier((slab, rows))
    n_pw = lax.axis_size("pw")
    slab = slab.reshape(bands_here, planes, 2, n_pw, planes, grid)
    piece = exchange(jnp.transpose(slab, (3, 0, 1, 2, 4, 5)), "pw")
    piece, rows = lax.optimization_barrier((piece, rows))
    piece = jnp.transpose(piece, (1, 0, 2, 3, 4, 5))
    piece = piece.reshape(bands_here, 2 * grid, planes, grid)
    piece = contract(piece, dft_table(grid, True, "kc", "nd"), "bwyz,wv->bvyz")
    piece = piece.reshape(bands_here, grid, 2, planes, grid) * potential[None, :, None]
    piece = piece.reshape(bands_here, 2 * grid, planes, grid)
    piece = contract(piece, dft_table(grid, False, "kc", "nd"), "bwyz,wv->bvyz")
    width = planes * 2 * planes * grid
    payload = piece.reshape(bands_here, n_pw, width).transpose(1, 0, 2)
    payload = payload.reshape(n_pw, bands_here * width)
    extra = jnp.broadcast_to(rows.reshape(1, -1), (n_pw, rows.size))
    payload = jnp.concatenate([payload, extra], axis=1)
    payload = lax.all_to_all(payload, "pw", split_axis=0, concat_axis=0, tiled=True)
    gram = jnp.sum(payload[:, bands_here * width :], axis=0).reshape(rows.shape)
    gram = gram / (columns * n_pw)
    back = payload[:, : bands_here * width].reshape(n_pw, bands_here, planes, 2, planes, grid)
    back = jnp.transpose(back, (1, 2, 3, 0, 4, 5))
    back = back.reshape(bands_here, planes, 2 * grid, grid)
    back = contract(back, dft_table(grid, False, "ck", "nd"), "bxwz,wv->bxvz")
    back = back.reshape(bands_here, planes, grid, 2 * grid)
    back = contract(back, dft_table(grid, False, "ck", "dn"), "bxyw,wv->bxyv")
    back = back.reshape(bands_here, planes, grid, 2, blocks, 8)
    picked = jnp.sum(jnp.where(hit[None, :, :, None], back, 0.0), axis=-1)
    applied = jnp.transpose(picked, (3, 0, 1, 2, 4)).reshape(2, bands_here, columns)
    return (applied, gram)


def solution(mesh):
    placed = (P(None, "band", "pw"), P("pw"), P(None, "pw", None))
    return jax.shard_map(
        local,
        mesh=mesh,
        in_specs=placed,
        out_specs=(P(None, "band", "pw"), P(None, "band", None)),
        check_vma=False,
    )
```

```python
import math

import jax
import numpy as np
import jax.numpy as jnp
from jax import lax
from jax.sharding import Mesh, PartitionSpec as P

HIGHEST = lax.Precision.HIGHEST


def dft_table(length, inverse, rows, cols):
    indices = np.arange(length)
    angles = (np.outer(indices, indices) % length) * (2.0 * np.pi / length)
    cos, sin = np.cos(angles), np.sin(angles)
    if inverse:
        cos, sin = cos / length, sin / length
        table = np.stack([np.stack([cos, sin], 1), np.stack([-sin, cos], 1)], 0)
    else:
        table = np.stack([np.stack([cos, -sin], 1), np.stack([sin, cos], 1)], 0)
    perm_in = (0, 1) if rows == "ck" else (1, 0)
    perm_out = (2, 3) if cols == "dn" else (3, 2)
    table = np.transpose(table, perm_in + perm_out)
    return jnp.asarray(table.reshape(2 * length, 2 * length).astype(np.float32))


def contract(values, table, form):
    return jnp.einsum(form, values, table, precision=HIGHEST)


def exchange(blocks, axis):
    n = blocks.shape[0]
    flat = lax.all_to_all(blocks.reshape(n, -1), axis, split_axis=0, concat_axis=0, tiled=True)
    return flat.reshape(blocks.shape)


def exchange_with_rows(blocks, rows, axis):
    n = blocks.shape[0]
    flat = blocks.reshape(n, -1)
    width = flat.shape[1]
    extra = jnp.broadcast_to(rows.reshape(1, -1), (n, rows.size))
    flat = jnp.concatenate([flat, extra], axis=1)
    flat = lax.all_to_all(flat, axis, split_axis=0, concat_axis=0, tiled=True)
    total = jnp.sum(flat[:, width:], axis=0).reshape(rows.shape)
    return flat[:, :width].reshape(blocks.shape), total


def gram_rows(orbitals):
    _, bands_here, columns = orbitals.shape
    n_band = lax.axis_size("band")
    chunk = columns // n_band
    pieces = orbitals.reshape(2, bands_here, n_band, chunk)
    pieces = lax.all_to_all(pieces, "band", split_axis=2, concat_axis=1, tiled=True)
    bands = bands_here * n_band
    stacked = pieces.reshape(2 * bands, chunk)
    prod = lax.dot_general(stacked, stacked, (((1,), (1,)), ((), ())), precision=HIGHEST)
    gram_real = prod[:bands, :bands] + prod[bands:, bands:]
    gram_imag = prod[:bands, bands:] - prod[bands:, :bands]
    partial = jnp.stack([gram_real, gram_imag]).reshape(1, 2, n_band, bands_here, bands)
    rows = lax.all_to_all(partial, "band", split_axis=2, concat_axis=0, tiled=True)
    return jnp.sum(rows, axis=0).reshape(2, bands_here, bands)


def local(orbitals, pw_index, potential):
    _, bands_here, columns = orbitals.shape
    grid = potential.shape[0]
    planes = potential.shape[1]
    blocks = grid // 8
    offsets = (pw_index - 8 * lax.iota(jnp.int32, columns)).reshape(planes, grid, blocks)
    lanes = lax.iota(jnp.int32, 8)
    hit = offsets[..., None] == lanes
    rows = gram_rows(orbitals)

    coeffs = orbitals.reshape(2, bands_here, planes, grid, blocks)
    coeffs = jnp.transpose(coeffs, (1, 2, 3, 0, 4))
    spread = jnp.where(hit[None, :, :, None], coeffs[..., None], 0.0)
    spread = spread.reshape(bands_here, planes, grid, 2 * grid)

    slab = contract(spread, dft_table(grid, True, "ck", "dn"), "bxyw,wv->bxyv")
    slab = slab.reshape(bands_here, planes, 2 * grid, grid)
    slab = contract(slab, dft_table(grid, True, "kc", "dn"), "bxwz,wv->bxvz")
    n_hi, n_lo = lax.axis_size("pw_hi"), lax.axis_size("pw_lo")
    slab = slab.reshape(bands_here, planes, 2, n_hi, n_lo, planes, grid)
    slab = exchange(jnp.transpose(slab, (4, 0, 1, 2, 3, 5, 6)), "pw_lo")
    slab = exchange(jnp.transpose(slab, (4, 0, 1, 2, 3, 5, 6)), "pw_hi")
    piece = jnp.transpose(slab, (2, 0, 1, 3, 4, 5, 6))
    piece = piece.reshape(bands_here, 2 * grid, planes, grid)
    piece = contract(piece, dft_table(grid, True, "kc", "nd"), "bwyz,wv->bvyz")
    piece = piece.reshape(bands_here, grid, 2, planes, grid) * potential[None, :, None]
    piece = piece.reshape(bands_here, 2 * grid, planes, grid)
    piece = contract(piece, dft_table(grid, False, "kc", "nd"), "bwyz,wv->bvyz")
    piece = piece.reshape(bands_here, n_hi, n_lo, planes, 2, planes, grid)
    piece, rows = exchange_with_rows(jnp.transpose(piece, (2, 0, 1, 3, 4, 5, 6)), rows, "pw_lo")
    piece, rows = exchange_with_rows(jnp.transpose(piece, (2, 0, 1, 3, 4, 5, 6)), rows, "pw_hi")
    gram = rows / (columns * n_hi * n_lo)
    back = jnp.transpose(piece, (2, 3, 4, 0, 1, 5, 6))
    back = back.reshape(bands_here, planes, 2 * grid, grid)
    back = contract(back, dft_table(grid, False, "ck", "nd"), "bxwz,wv->bxvz")
    back = back.reshape(bands_here, planes, grid, 2 * grid)
    back = contract(back, dft_table(grid, False, "ck", "dn"), "bxyw,wv->bxyv")
    back = back.reshape(bands_here, planes, grid, 2, blocks, 8)
    picked = jnp.sum(jnp.where(hit[None, :, :, None], back, 0.0), axis=-1)
    applied = jnp.transpose(picked, (3, 0, 1, 2, 4)).reshape(2, bands_here, columns)
    return (applied, gram)


def solution(mesh):
    n_band, n_pw = mesh.devices.shape
    n_hi = 4 if n_pw % 4 == 0 else 1
    fine = Mesh(mesh.devices.reshape(n_band, n_hi, n_pw // n_hi), ("band", "pw_hi", "pw_lo"))
    pw = ("pw_hi", "pw_lo")
    placed = (P(None, "band", pw), P(pw), P(None, pw, None))
    return jax.shard_map(
        local,
        mesh=fine,
        in_specs=placed,
        out_specs=(P(None, "band", pw), P(None, "band", None)),
        check_vma=False,
    )
```

```python
import math

import jax
import numpy as np
import jax.numpy as jnp
from jax import lax
from jax.sharding import PartitionSpec as P

HIGHEST = lax.Precision.HIGHEST


def dft_table(length, inverse, rows, cols):
    indices = np.arange(length)
    angles = (np.outer(indices, indices) % length) * (2.0 * np.pi / length)
    cos, sin = np.cos(angles), np.sin(angles)
    if inverse:
        cos, sin = cos / length, sin / length
        table = np.stack([np.stack([cos, sin], 1), np.stack([-sin, cos], 1)], 0)
    else:
        table = np.stack([np.stack([cos, -sin], 1), np.stack([sin, cos], 1)], 0)
    perm_in = (0, 1) if rows == "ck" else (1, 0)
    perm_out = (2, 3) if cols == "dn" else (3, 2)
    table = np.transpose(table, perm_in + perm_out)
    return table.reshape(2 * length, 2 * length).astype(np.float32)


def contract(values, table, form):
    return jnp.einsum(form, values, table, precision=HIGHEST)


def gram_rows(orbitals):
    _, bands_here, columns = orbitals.shape
    n_band = lax.axis_size("band")
    chunk = columns // n_band
    pieces = orbitals.reshape(2, bands_here, n_band, chunk)
    pieces = lax.all_to_all(pieces, "band", split_axis=2, concat_axis=1, tiled=True)
    bands = bands_here * n_band
    stacked = pieces.reshape(2 * bands, chunk)
    prod = lax.dot_general(stacked, stacked, (((1,), (1,)), ((), ())), precision=HIGHEST)
    gram_real = prod[:bands, :bands] + prod[bands:, bands:]
    gram_imag = prod[:bands, bands:] - prod[bands:, :bands]
    partial = jnp.stack([gram_real, gram_imag]).reshape(1, 2, n_band, bands_here, bands)
    rows = lax.all_to_all(partial, "band", split_axis=2, concat_axis=0, tiled=True)
    return jnp.sum(rows, axis=0).reshape(2, bands_here, bands)


def local(orbitals, pw_index, potential):
    _, bands_here, columns = orbitals.shape
    grid = potential.shape[0]
    planes = potential.shape[1]
    blocks = grid // 8
    offsets = (pw_index - 8 * lax.iota(jnp.int32, columns)).reshape(planes, grid, blocks)
    lanes = lax.iota(jnp.int32, 8)
    hit = offsets[..., None] == lanes
    rows = gram_rows(orbitals)
    kinds = [(True, "ck", "dn"), (True, "kc", "dn"), (True, "kc", "nd"),
             (False, "kc", "nd"), (False, "ck", "nd"), (False, "ck", "dn")]
    tables = jnp.asarray(np.stack([dft_table(grid, *kind) for kind in kinds]))
    tables = lax.optimization_barrier(tables)

    coeffs = orbitals.reshape(2, bands_here, planes, grid, blocks)
    coeffs = jnp.transpose(coeffs, (1, 2, 3, 0, 4))
    spread = jnp.where(hit[None, :, :, None], coeffs[..., None], 0.0)
    spread = spread.reshape(bands_here, planes, grid, 2 * grid)

    slab = contract(spread, tables[0], "bxyw,wv->bxyv")
    slab = slab.reshape(bands_here, planes, 2 * grid, grid)
    slab = contract(slab, tables[1], "bxwz,wv->bxvz")
    slab = slab.reshape(bands_here, planes, 2, grid, grid)
    piece = lax.all_to_all(slab, "pw", split_axis=3, concat_axis=1, tiled=True)
    piece = piece.reshape(bands_here, 2 * grid, planes, grid)
    piece = contract(piece, tables[2], "bwyz,wv->bvyz")
    piece = piece.reshape(bands_here, grid, 2, planes, grid) * potential[None, :, None]
    piece = piece.reshape(bands_here, 2 * grid, planes, grid)
    piece = contract(piece, tables[3], "bwyz,wv->bvyz")
    n_pw = lax.axis_size("pw")
    width = planes * 2 * planes * grid
    payload = piece.reshape(bands_here, n_pw, width).transpose(1, 0, 2)
    payload = payload.reshape(n_pw, bands_here * width)
    extra = jnp.broadcast_to(rows.reshape(1, -1), (n_pw, rows.size))
    payload = jnp.concatenate([payload, extra], axis=1)
    payload = lax.all_to_all(payload, "pw", split_axis=0, concat_axis=0, tiled=True)
    gram = jnp.sum(payload[:, bands_here * width :], axis=0).reshape(rows.shape)
    gram = gram / (columns * n_pw)
    back = payload[:, : bands_here * width].reshape(n_pw, bands_here, planes, 2, planes, grid)
    back = jnp.transpose(back, (1, 2, 3, 0, 4, 5))
    back = back.reshape(bands_here, planes, 2 * grid, grid)
    back = contract(back, tables[4], "bxwz,wv->bxvz")
    back = back.reshape(bands_here, planes, grid, 2 * grid)
    back = contract(back, tables[5], "bxyw,wv->bxyv")
    back = back.reshape(bands_here, planes, grid, 2, blocks, 8)
    picked = jnp.sum(jnp.where(hit[None, :, :, None], back, 0.0), axis=-1)
    applied = jnp.transpose(picked, (3, 0, 1, 2, 4)).reshape(2, bands_here, columns)
    return (applied, gram)


def solution(mesh):
    placed = (P(None, "band", "pw"), P("pw"), P(None, "pw", None))
    return jax.shard_map(
        local,
        mesh=mesh,
        in_specs=placed,
        out_specs=(P(None, "band", "pw"), P(None, "band", None)),
        check_vma=False,
    )
```

```python
import math

import jax
import numpy as np
import jax.numpy as jnp
from jax import lax
from jax.sharding import PartitionSpec as P

HIGHEST = lax.Precision.HIGHEST


def dft_table(length, inverse, rows, cols):
    indices = np.arange(length)
    angles = (np.outer(indices, indices) % length) * (2.0 * np.pi / length)
    cos, sin = np.cos(angles), np.sin(angles)
    if inverse:
        cos, sin = cos / length, sin / length
        table = np.stack([np.stack([cos, sin], 1), np.stack([-sin, cos], 1)], 0)
    else:
        table = np.stack([np.stack([cos, -sin], 1), np.stack([sin, cos], 1)], 0)
    perm_in = (0, 1) if rows == "ck" else (1, 0)
    perm_out = (2, 3) if cols == "dn" else (3, 2)
    table = np.transpose(table, perm_in + perm_out)
    return table.reshape(2 * length, 2 * length).astype(np.float32)


def contract(values, table, form):
    return jnp.einsum(form, values, table, precision=HIGHEST)


def gram_rows(orbitals):
    _, bands_here, columns = orbitals.shape
    n_band = lax.axis_size("band")
    chunk = columns // n_band
    pieces = lax.all_to_all(orbitals, "band", split_axis=2, concat_axis=2, tiled=True)
    pieces = jnp.transpose(pieces.reshape(2, bands_here, n_band, chunk), (0, 2, 1, 3))
    bands = bands_here * n_band
    stacked = pieces.reshape(2 * bands, chunk)
    prod = lax.dot_general(stacked, stacked, (((1,), (1,)), ((), ())), precision=HIGHEST)
    gram_real = prod[:bands, :bands] + prod[bands:, bands:]
    gram_imag = prod[:bands, bands:] - prod[bands:, :bands]
    partial = jnp.stack([gram_real, gram_imag])
    rows = lax.all_to_all(partial, "band", split_axis=1, concat_axis=1, tiled=True)
    rows = rows.reshape(2, n_band, bands_here, bands)
    return jnp.sum(rows, axis=1)


def local(orbitals, pw_index, potential):
    _, bands_here, columns = orbitals.shape
    grid = potential.shape[0]
    planes = potential.shape[1]
    blocks = grid // 8
    offsets = (pw_index - 8 * lax.iota(jnp.int32, columns)).reshape(planes, grid, blocks)
    lanes = lax.iota(jnp.int32, 8)
    hit = offsets[..., None] == lanes
    rows = gram_rows(orbitals)
    kinds = [(True, "ck", "dn"), (True, "kc", "dn"), (True, "kc", "nd"),
             (False, "kc", "nd"), (False, "ck", "nd"), (False, "ck", "dn")]
    tables = jnp.asarray(np.stack([dft_table(grid, *kind) for kind in kinds]))
    tables = lax.optimization_barrier(tables)

    coeffs = orbitals.reshape(2, bands_here, planes, grid, blocks)
    coeffs = jnp.transpose(coeffs, (1, 2, 3, 0, 4))
    spread = jnp.where(hit[None, :, :, None], coeffs[..., None], 0.0)
    spread = spread.reshape(bands_here, planes, grid, 2 * grid)

    slab = contract(spread, tables[0], "bxyw,wv->bxyv")
    slab = slab.reshape(bands_here, planes, 2 * grid, grid)
    slab = contract(slab, tables[1], "bxwz,wv->bxvz")
    slab = slab.reshape(bands_here, planes, 2, grid, grid)
    piece = lax.all_to_all(slab, "pw", split_axis=3, concat_axis=1, tiled=True)
    piece = piece.reshape(bands_here, 2 * grid, planes, grid)
    piece = contract(piece, tables[2], "bwyz,wv->bvyz")
    piece = piece.reshape(bands_here, grid, 2, planes, grid) * potential[None, :, None]
    piece = piece.reshape(bands_here, 2 * grid, planes, grid)
    piece = contract(piece, tables[3], "bwyz,wv->bvyz")
    n_pw = lax.axis_size("pw")
    width = planes * 2 * planes * grid
    payload = piece.reshape(bands_here, n_pw, width).transpose(1, 0, 2)
    payload = payload.reshape(n_pw, bands_here * width)
    extra = jnp.broadcast_to(rows.reshape(1, -1), (n_pw, rows.size))
    payload = jnp.concatenate([payload, extra], axis=1)
    payload = lax.all_to_all(payload, "pw", split_axis=0, concat_axis=0, tiled=True)
    gram = jnp.sum(payload[:, bands_here * width :], axis=0).reshape(rows.shape)
    gram = gram / (columns * n_pw)
    back = payload[:, : bands_here * width].reshape(n_pw, bands_here, planes, 2, planes, grid)
    back = jnp.transpose(back, (1, 2, 3, 0, 4, 5))
    back = back.reshape(bands_here, planes, 2 * grid, grid)
    back = contract(back, tables[4], "bxwz,wv->bxvz")
    back = back.reshape(bands_here, planes, grid, 2 * grid)
    back = contract(back, tables[5], "bxyw,wv->bxyv")
    back = back.reshape(bands_here, planes, grid, 2, blocks, 8)
    picked = jnp.sum(jnp.where(hit[None, :, :, None], back, 0.0), axis=-1)
    applied = jnp.transpose(picked, (3, 0, 1, 2, 4)).reshape(2, bands_here, columns)
    return (applied, gram)


def solution(mesh):
    placed = (P(None, "band", "pw"), P("pw"), P(None, "pw", None))
    return jax.shard_map(
        local,
        mesh=mesh,
        in_specs=placed,
        out_specs=(P(None, "band", "pw"), P(None, "band", None)),
        check_vma=False,
    )
```

```python
import math

import jax
import numpy as np
import jax.numpy as jnp
from jax import lax
from jax.sharding import PartitionSpec as P

HIGHEST = lax.Precision.HIGHEST


def dft_table(length, inverse, rows, cols):
    indices = np.arange(length)
    angles = (np.outer(indices, indices) % length) * (2.0 * np.pi / length)
    cos, sin = np.cos(angles), np.sin(angles)
    if inverse:
        cos, sin = cos / length, sin / length
        table = np.stack([np.stack([cos, sin], 1), np.stack([-sin, cos], 1)], 0)
    else:
        table = np.stack([np.stack([cos, -sin], 1), np.stack([sin, cos], 1)], 0)
    perm_in = (0, 1) if rows == "ck" else (1, 0)
    perm_out = (2, 3) if cols == "dn" else (3, 2)
    table = np.transpose(table, perm_in + perm_out)
    return table.reshape(2 * length, 2 * length).astype(np.float32)


def contract(values, table, form):
    return jnp.einsum(form, values, table, precision=HIGHEST)


def gram_rows(orbitals):
    _, bands_here, columns = orbitals.shape
    n_band = lax.axis_size("band")
    chunk = columns // n_band
    pieces = orbitals.reshape(2, bands_here, n_band, chunk)
    pieces = lax.all_to_all(pieces, "band", split_axis=2, concat_axis=1, tiled=True)
    bands = bands_here * n_band
    stacked = pieces.reshape(2 * bands, chunk)
    prod = lax.dot_general(stacked, stacked, (((1,), (1,)), ((), ())), precision=HIGHEST)
    gram_real = prod[:bands, :bands] + prod[bands:, bands:]
    gram_imag = prod[:bands, bands:] - prod[bands:, :bands]
    partial = jnp.stack([gram_real, gram_imag]).reshape(1, 2, n_band, bands_here, bands)
    rows = lax.all_to_all(partial, "band", split_axis=2, concat_axis=0, tiled=True)
    return jnp.sum(rows, axis=0).reshape(2, bands_here, bands)


def local(orbitals, pw_index, potential):
    _, bands_here, columns = orbitals.shape
    grid = potential.shape[0]
    planes = potential.shape[1]
    blocks = grid // 8
    offsets = (pw_index - 8 * lax.iota(jnp.int32, columns)).reshape(planes, grid, blocks)
    lanes = lax.iota(jnp.int32, 8)
    hit = offsets[..., None] == lanes
    rows = gram_rows(orbitals)
    kinds = [(True, "ck", "dn"), (True, "kc", "dn"), (True, "kc", "nd"),
             (False, "kc", "nd"), (False, "ck", "nd"), (False, "ck", "dn")]
    tables = jnp.asarray(np.stack([dft_table(grid, *kind) for kind in kinds]))
    tables = lax.optimization_barrier(tables)

    coeffs = orbitals.reshape(2, bands_here, planes, grid, blocks)
    coeffs = jnp.transpose(coeffs, (1, 2, 3, 0, 4))
    spread = jnp.where(hit[None, :, :, None], coeffs[..., None], 0.0)
    spread = spread.reshape(bands_here, planes, grid, 2 * grid)

    slab = contract(spread, tables[0], "bxyw,wv->bxyv")
    slab = slab.reshape(bands_here, planes, 2 * grid, grid)
    slab = contract(slab, tables[1], "bxwz,wv->bxvz")
    slab = slab.reshape(bands_here, planes, 2, grid, grid)
    piece = lax.all_to_all(slab, "pw", split_axis=3, concat_axis=1, tiled=True)
    piece = piece.reshape(bands_here, 2 * grid, planes, grid)
    piece = contract(piece, tables[2], "bwyz,wv->bvyz")
    piece = piece.reshape(bands_here, grid, 2, planes, grid) * potential[None, :, None]
    piece = piece.reshape(bands_here, 2 * grid, planes, grid)
    piece = contract(piece, tables[3], "bwyz,wv->bvyz")
    n_pw = lax.axis_size("pw")
    width = planes * 2 * planes * grid
    payload = piece.reshape(bands_here, n_pw, width).transpose(1, 0, 2)
    payload = payload.reshape(n_pw, bands_here * width)
    extra = jnp.broadcast_to(rows.reshape(1, -1), (n_pw, rows.size))
    payload = jnp.concatenate([payload, extra], axis=1)
    length = payload.shape[1]
    if length % 128 == 0:
        payload = payload.reshape(n_pw, length // 128, 128)
    payload = lax.all_to_all(payload, "pw", split_axis=0, concat_axis=0, tiled=True)
    payload = payload.reshape(n_pw, length)
    gram = jnp.sum(payload[:, bands_here * width :], axis=0).reshape(rows.shape)
    gram = gram / (columns * n_pw)
    back = payload[:, : bands_here * width].reshape(n_pw, bands_here, planes, 2, planes, grid)
    back = jnp.transpose(back, (1, 2, 3, 0, 4, 5))
    back = back.reshape(bands_here, planes, 2 * grid, grid)
    back = contract(back, tables[4], "bxwz,wv->bxvz")
    back = back.reshape(bands_here, planes, grid, 2 * grid)
    back = contract(back, tables[5], "bxyw,wv->bxyv")
    back = back.reshape(bands_here, planes, grid, 2, blocks, 8)
    picked = jnp.sum(jnp.where(hit[None, :, :, None], back, 0.0), axis=-1)
    applied = jnp.transpose(picked, (3, 0, 1, 2, 4)).reshape(2, bands_here, columns)
    return (applied, gram)


def solution(mesh):
    placed = (P(None, "band", "pw"), P("pw"), P(None, "pw", None))
    return jax.shard_map(
        local,
        mesh=mesh,
        in_specs=placed,
        out_specs=(P(None, "band", "pw"), P(None, "band", None)),
        check_vma=False,
    )
```

```python
import math

import jax
import numpy as np
import jax.numpy as jnp
from jax import lax
from jax.sharding import PartitionSpec as P

HIGHEST = lax.Precision.HIGHEST


def dft_table(length, inverse, rows, cols):
    indices = np.arange(length)
    angles = (np.outer(indices, indices) % length) * (2.0 * np.pi / length)
    cos, sin = np.cos(angles), np.sin(angles)
    if inverse:
        cos, sin = cos / length, sin / length
        table = np.stack([np.stack([cos, sin], 1), np.stack([-sin, cos], 1)], 0)
    else:
        table = np.stack([np.stack([cos, -sin], 1), np.stack([sin, cos], 1)], 0)
    perm_in = (0, 1) if rows == "ck" else (1, 0)
    perm_out = (2, 3) if cols == "dn" else (3, 2)
    table = np.transpose(table, perm_in + perm_out)
    return table.reshape(2 * length, 2 * length).astype(np.float32)


def contract(values, table, form):
    return jnp.einsum(form, values, table, precision=HIGHEST)


def gram_rows(orbitals):
    _, bands_here, columns = orbitals.shape
    n_band = lax.axis_size("band")
    chunk = columns // n_band
    pieces = orbitals.reshape(2, bands_here, n_band, chunk)
    pieces = lax.all_to_all(pieces, "band", split_axis=2, concat_axis=1, tiled=True)
    bands = bands_here * n_band
    stacked = pieces.reshape(2 * bands, chunk)
    prod = lax.dot_general(stacked, stacked, (((1,), (1,)), ((), ())), precision=HIGHEST)
    gram_real = prod[:bands, :bands] + prod[bands:, bands:]
    gram_imag = prod[:bands, bands:] - prod[bands:, :bands]
    return jnp.stack([gram_real, gram_imag]).reshape(1, 2, n_band, bands_here, bands)


def scatter_rows(partial):
    _, _, _, bands_here, bands = partial.shape
    rows = lax.all_to_all(partial, "band", split_axis=2, concat_axis=0, tiled=True)
    return jnp.sum(rows, axis=0).reshape(2, bands_here, bands)


def local(orbitals, pw_index, potential):
    _, bands_here, columns = orbitals.shape
    grid = potential.shape[0]
    planes = potential.shape[1]
    blocks = grid // 8
    offsets = (pw_index - 8 * lax.iota(jnp.int32, columns)).reshape(planes, grid, blocks)
    lanes = lax.iota(jnp.int32, 8)
    hit = offsets[..., None] == lanes
    partial = gram_rows(orbitals)
    kinds = [(True, "ck", "dn"), (True, "kc", "dn"), (True, "kc", "nd"),
             (False, "kc", "nd"), (False, "ck", "nd"), (False, "ck", "dn")]
    tables = jnp.asarray(np.stack([dft_table(grid, *kind) for kind in kinds]))
    tables = lax.optimization_barrier(tables)

    coeffs = orbitals.reshape(2, bands_here, planes, grid, blocks)
    coeffs = jnp.transpose(coeffs, (1, 2, 3, 0, 4))
    spread = jnp.where(hit[None, :, :, None], coeffs[..., None], 0.0)
    spread = spread.reshape(bands_here, planes, grid, 2 * grid)

    slab = contract(spread, tables[0], "bxyw,wv->bxyv")
    slab = slab.reshape(bands_here, planes, 2 * grid, grid)
    slab = contract(slab, tables[1], "bxwz,wv->bxvz")
    slab = slab.reshape(bands_here, planes, 2, grid, grid)
    piece = lax.all_to_all(slab, "pw", split_axis=3, concat_axis=1, tiled=True)
    piece, partial = lax.optimization_barrier((piece, partial))
    rows = scatter_rows(partial)
    piece = piece.reshape(bands_here, 2 * grid, planes, grid)
    piece = contract(piece, tables[2], "bwyz,wv->bvyz")
    piece = piece.reshape(bands_here, grid, 2, planes, grid) * potential[None, :, None]
    piece = piece.reshape(bands_here, 2 * grid, planes, grid)
    piece = contract(piece, tables[3], "bwyz,wv->bvyz")
    n_pw = lax.axis_size("pw")
    width = planes * 2 * planes * grid
    payload = piece.reshape(bands_here, n_pw, width).transpose(1, 0, 2)
    payload = payload.reshape(n_pw, bands_here * width)
    extra = jnp.broadcast_to(rows.reshape(1, -1), (n_pw, rows.size))
    payload = jnp.concatenate([payload, extra], axis=1)
    payload = lax.all_to_all(payload, "pw", split_axis=0, concat_axis=0, tiled=True)
    gram = jnp.sum(payload[:, bands_here * width :], axis=0).reshape(rows.shape)
    gram = gram / (columns * n_pw)
    back = payload[:, : bands_here * width].reshape(n_pw, bands_here, planes, 2, planes, grid)
    back = jnp.transpose(back, (1, 2, 3, 0, 4, 5))
    back = back.reshape(bands_here, planes, 2 * grid, grid)
    back = contract(back, tables[4], "bxwz,wv->bxvz")
    back = back.reshape(bands_here, planes, grid, 2 * grid)
    back = contract(back, tables[5], "bxyw,wv->bxyv")
    back = back.reshape(bands_here, planes, grid, 2, blocks, 8)
    picked = jnp.sum(jnp.where(hit[None, :, :, None], back, 0.0), axis=-1)
    applied = jnp.transpose(picked, (3, 0, 1, 2, 4)).reshape(2, bands_here, columns)
    return (applied, gram)


def solution(mesh):
    placed = (P(None, "band", "pw"), P("pw"), P(None, "pw", None))
    return jax.shard_map(
        local,
        mesh=mesh,
        in_specs=placed,
        out_specs=(P(None, "band", "pw"), P(None, "band", None)),
        check_vma=False,
    )
```

```python
import math

import jax
import numpy as np
import jax.numpy as jnp
from jax import lax
from jax.sharding import PartitionSpec as P

HIGHEST = lax.Precision.HIGHEST


def dft_table(length, inverse, rows, cols):
    indices = np.arange(length)
    angles = (np.outer(indices, indices) % length) * (2.0 * np.pi / length)
    cos, sin = np.cos(angles), np.sin(angles)
    if inverse:
        cos, sin = cos / length, sin / length
        table = np.stack([np.stack([cos, sin], 1), np.stack([-sin, cos], 1)], 0)
    else:
        table = np.stack([np.stack([cos, -sin], 1), np.stack([sin, cos], 1)], 0)
    perm_in = (0, 1) if rows == "ck" else (1, 0)
    perm_out = (2, 3) if cols == "dn" else (3, 2)
    table = np.transpose(table, perm_in + perm_out)
    return table.reshape(2 * length, 2 * length).astype(np.float32)


def contract(values, table, form):
    return jnp.einsum(form, values, table, precision=HIGHEST)


def gram_rows(orbitals):
    _, bands_here, columns = orbitals.shape
    n_band = lax.axis_size("band")
    chunk = columns // n_band
    pieces = orbitals.reshape(2, bands_here, n_band, chunk)
    pieces = lax.all_to_all(pieces, "band", split_axis=2, concat_axis=1, tiled=True)
    bands = bands_here * n_band
    stacked = pieces.reshape(2 * bands, chunk)
    prod = lax.dot_general(stacked, stacked, (((1,), (1,)), ((), ())), precision=HIGHEST)
    gram_real = prod[:bands, :bands] + prod[bands:, bands:]
    gram_imag = prod[:bands, bands:] - prod[bands:, :bands]
    return jnp.stack([gram_real, gram_imag]).reshape(1, 2, n_band, bands_here, bands)


def scatter_rows(partial):
    _, _, _, bands_here, bands = partial.shape
    rows = lax.all_to_all(partial, "band", split_axis=2, concat_axis=0, tiled=True)
    return jnp.sum(rows, axis=0).reshape(2, bands_here, bands)


def local(orbitals, pw_index, potential):
    _, bands_here, columns = orbitals.shape
    grid = potential.shape[0]
    planes = potential.shape[1]
    blocks = grid // 8
    offsets = (pw_index - 8 * lax.iota(jnp.int32, columns)).reshape(planes, grid, blocks)
    lanes = lax.iota(jnp.int32, 8)
    hit = offsets[..., None] == lanes
    partial = gram_rows(orbitals)
    kinds = [(True, "ck", "dn"), (True, "kc", "dn"), (True, "kc", "nd"),
             (False, "kc", "nd"), (False, "ck", "nd"), (False, "ck", "dn")]
    tables = jnp.asarray(np.stack([dft_table(grid, *kind) for kind in kinds]))
    tables = lax.optimization_barrier(tables)

    coeffs = orbitals.reshape(2, bands_here, planes, grid, blocks)
    coeffs = jnp.transpose(coeffs, (1, 2, 3, 0, 4))
    spread = jnp.where(hit[None, :, :, None], coeffs[..., None], 0.0)
    spread = spread.reshape(bands_here, planes, grid, 2 * grid)

    slab = contract(spread, tables[0], "bxyw,wv->bxyv")
    slab = slab.reshape(bands_here, planes, 2 * grid, grid)
    slab = contract(slab, tables[1], "bxwz,wv->bxvz")
    slab = slab.reshape(bands_here, planes, 2, grid, grid)
    piece = lax.all_to_all(slab, "pw", split_axis=3, concat_axis=1, tiled=True)
    piece, partial = lax.optimization_barrier((piece, partial))
    rows = scatter_rows(partial)
    piece = piece.reshape(bands_here, 2 * grid, planes, grid)
    piece = contract(piece, tables[2], "bwyz,wv->bvyz")
    piece = piece.reshape(bands_here, grid, 2, planes, grid) * potential[None, :, None]
    piece = piece.reshape(bands_here, 2 * grid, planes, grid)
    piece = contract(piece, tables[3], "bwyz,wv->bvyz")
    n_pw = lax.axis_size("pw")
    width = planes * 2 * planes * grid
    payload = piece.reshape(bands_here, n_pw, width).transpose(1, 0, 2)
    payload = payload.reshape(n_pw, bands_here * width)
    payload = jnp.concatenate([payload, jnp.zeros((n_pw, rows.size), payload.dtype)], axis=1)
    payload = lax.optimization_barrier(payload)
    extra = jnp.broadcast_to(rows.reshape(1, -1), (n_pw, rows.size))
    payload = lax.dynamic_update_slice(payload, extra, (0, bands_here * width))
    payload = lax.all_to_all(payload, "pw", split_axis=0, concat_axis=0, tiled=True)
    gram = jnp.sum(payload[:, bands_here * width :], axis=0).reshape(rows.shape)
    gram = gram / (columns * n_pw)
    back = payload[:, : bands_here * width].reshape(n_pw, bands_here, planes, 2, planes, grid)
    back = jnp.transpose(back, (1, 2, 3, 0, 4, 5))
    back = back.reshape(bands_here, planes, 2 * grid, grid)
    back = contract(back, tables[4], "bxwz,wv->bxvz")
    back = back.reshape(bands_here, planes, grid, 2 * grid)
    back = contract(back, tables[5], "bxyw,wv->bxyv")
    back = back.reshape(bands_here, planes, grid, 2, blocks, 8)
    picked = jnp.sum(jnp.where(hit[None, :, :, None], back, 0.0), axis=-1)
    applied = jnp.transpose(picked, (3, 0, 1, 2, 4)).reshape(2, bands_here, columns)
    return (applied, gram)


def solution(mesh):
    placed = (P(None, "band", "pw"), P("pw"), P(None, "pw", None))
    return jax.shard_map(
        local,
        mesh=mesh,
        in_specs=placed,
        out_specs=(P(None, "band", "pw"), P(None, "band", None)),
        check_vma=False,
    )
```
